256 devices in a mesh: ctx: 32 (over y, z), tp: 8 (over x, core).
Axes of the slice: x: 4, y: 4, z: 8, core: 2. Of those that a mesh axis runs over, the one named last changes fastest.
Arguments:
- tokens: bfloat16 [16384, 4096], P('ctx', 'tp'), may hold values from -6 to 6
- qkv_blocks: bfloat16 [3, 4, 1024, 1024], P(None, None, None, 'tp'), may hold values from -0.046875 to 0.046875
- out_blocks: bfloat16 [4, 1024, 1024], P(None, 'tp'), may hold values from -0.046875 to 0.046875
- mix_factors: float32 [4, 4, 4, 4], replicated, may hold values from -4 to 4
- head_gain: float32 [4, 1024], P(None, 'tp'), may hold values from 0.1 to 1.9
Outputs:
- layer_out: bfloat16 [16384, 4096], P('ctx', 'tp')
The draws below stay inside these ranges and needn't reach their ends.
All inputs are finite; a program needn't handle non-finite values.
Results may differ from the reference program's by a relative error of at most 0.025.
Values may be sent and summed in bfloat16 or wider, within the bound.
No kernel may reach another device: no remote copies, remote signals or barrier semaphores. Data moves between devices by JAX's collectives and lax.ppermute only.
A program may use at most 128 MiB of HBM per device.

```python
import jax
import jax.numpy as jnp
from jax import lax

D = 4096
HEADS = 32
PHM = 4
SPAN = 128
HEAD = 128
BLOCK = 1024
SEQ = 16384
N_TP = 8


def shard_levels(own_key, dims, split, low, high):
    def one(position, shards_of):
        draws = jax.random.uniform(jax.random.fold_in(jax.random.fold_in(own_key, 6), position), (shards_of,), jnp.float32, low / len(split), high / len(split))
        return jnp.repeat(jnp.exp(draws), dims[position] // shards_of).reshape((-1,) + (1,) * (len(dims) - position - 1))

    loudness = one(*split[0])
    for cut in split[1:]:
        loudness = loudness * one(*cut)
    return loudness


def gaussian(rng, dims, width, limit, cuts=(), dtype=jnp.bfloat16):
    entries = width * jax.random.normal(rng, dims, jnp.float32)
    if cuts:
        entries = entries * shard_levels(rng, dims, cuts, -0.22, 0.18)
    return jnp.clip(entries, -limit, limit).astype(dtype)


def setup_inputs(seed: int = 0) -> dict:
    arg_keys = jax.random.split(jax.random.key(seed), 6)
    return {
        "tokens": gaussian(arg_keys[0], (SEQ, D), 1.0, 6.0, ((0, 32), (1, 8))),
        "qkv_blocks": gaussian(arg_keys[1], (3, PHM, BLOCK, BLOCK), (4 * D) ** -0.5, 0.046875, ((3, 8),)),
        "out_blocks": gaussian(arg_keys[2], (PHM, BLOCK, BLOCK), (4 * D) ** -0.5, 0.046875, ((1, 8),)),
        "mix_factors": gaussian(arg_keys[3], (4, PHM, PHM, PHM), 1.0, 4.0, (), jnp.float32),
        "head_gain": jnp.clip(1.0 + 0.18 * jax.random.normal(arg_keys[4], (PHM, BLOCK), jnp.float32), 0.1, 1.9),
    }


epsilon = 1e-06

def project(inputs, blocks, mixing):
    tok_rows = inputs.shape[0]
    blocked = inputs.reshape(tok_rows * PHM, BLOCK)
    summed = jnp.zeros((tok_rows, PHM, BLOCK), jnp.float32)
    for term_index in range(PHM):
        product = jnp.dot(blocked, blocks[term_index], preferred_element_type=jnp.float32).reshape(tok_rows, PHM, BLOCK)
        summed = summed + jnp.einsum('tcg,cr->trg', product, mixing[term_index])
    return summed.reshape(tok_rows, D)

def reference(tokens, qkv_blocks, out_blocks, mix_factors, head_gain):
    nblk = SEQ // SPAN
    query_heads = project(tokens, qkv_blocks[0], mix_factors[0]).astype(jnp.bfloat16)
    key_heads = project(tokens, qkv_blocks[1], mix_factors[1]).astype(jnp.bfloat16)
    value_heads = project(tokens, qkv_blocks[2], mix_factors[2]).astype(jnp.bfloat16)
    query_f = query_heads.astype(jnp.float32).reshape(nblk, SPAN, HEADS, HEAD)
    key_f = key_heads.astype(jnp.float32).reshape(nblk, SPAN, HEADS, HEAD)
    value_f = value_heads.astype(jnp.float32).reshape(nblk, SPAN, HEADS, HEAD)
    states = jnp.einsum('nshd,nshe->nhde', key_f, value_f)
    running = jnp.cumsum(states, axis=0)
    prefix = jnp.concatenate([jnp.zeros_like(states[:1]), running[:-1]], axis=0)
    scores = jnp.einsum('nshd,nthd->nhst', query_f, key_f)
    causal = jnp.arange(SPAN)[:, None] >= jnp.arange(SPAN)[None, :]
    scores = jnp.where(causal[None, None], scores, 0.0).astype(jnp.bfloat16)
    within = jnp.einsum('nhst,nthe->nshe', scores.astype(jnp.float32), value_f)
    carried_out = jnp.einsum('nshd,nhde->nshe', query_f, prefix, precision=lax.Precision.HIGHEST)
    combined = within + carried_out
    mean_sq = lax.optimization_barrier(jnp.mean(combined * combined, axis=-1, keepdims=True))
    normed = combined * lax.rsqrt(mean_sq + epsilon) * head_gain.reshape(HEADS, HEAD)
    attn = normed.astype(jnp.bfloat16).reshape(SEQ, PHM, BLOCK)
    col_width = BLOCK // N_TP
    summed = jnp.zeros((SEQ, D), jnp.float32)
    for group_index in range(N_TP):
        columns = attn[:, :, group_index * col_width:(group_index + 1) * col_width].reshape(SEQ * PHM, col_width)
        partial_value = jnp.zeros((SEQ, PHM, BLOCK), jnp.float32)
        for term_index in range(PHM):
            rows_block = out_blocks[term_index, group_index * col_width:(group_index + 1) * col_width, :]
            product = jnp.dot(columns, rows_block, preferred_element_type=jnp.float32).reshape(SEQ, PHM, BLOCK)
            partial_value = partial_value + jnp.einsum('tch,cr->trh', product, mix_factors[3, term_index])
        rounded = lax.optimization_barrier(partial_value.reshape(SEQ, D).astype(jnp.bfloat16))
        summed = summed + rounded.astype(jnp.float32)
    return summed.astype(jnp.bfloat16)
```

```python
import functools

import jax
import jax.numpy as jnp
from jax import lax
from jax.sharding import PartitionSpec as P

PHM = 4
SPAN = 128
HEAD = 128
BLOCK = 1024


epsilon = 1e-06


def exclusive_prefix(value, axis, devices):
    acc = value
    shift = 1
    while shift < devices:
        pairs = [(i, i + shift) for i in range(devices - shift)]
        acc = acc + lax.ppermute(acc, axis, pairs)
        shift *= 2
    return acc - value


def fold_weights(blocks, mixing):
    terms, rows, cols = blocks.shape
    folded = None
    for term_index in range(terms):
        part = (
            mixing[term_index][:, None, :, None]
            * blocks[term_index].astype(jnp.float32)[None, :, None, :]
        )
        folded = part if folded is None else folded + part
    return folded.astype(jnp.bfloat16).reshape(PHM * rows, PHM * cols)


def on_device(ctx_devices, tokens, qkv_blocks, out_blocks, mix_factors, head_gain):
    col_width = qkv_blocks.shape[-1]
    w_qkv = [fold_weights(qkv_blocks[p], mix_factors[p]) for p in range(3)]
    w_out = fold_weights(out_blocks, mix_factors[3])

    whole = lax.all_gather(tokens, "tp", axis=1, tiled=True)
    tok_rows = whole.shape[0]
    local_heads = PHM * col_width // HEAD
    nblk = tok_rows // SPAN

    def project(p):
        out = jnp.dot(whole, w_qkv[p], preferred_element_type=jnp.float32)
        return out.astype(jnp.bfloat16).reshape(nblk, SPAN, local_heads, HEAD)

    key_heads = project(1)
    value_heads = project(2)
    states = jnp.einsum(
        "nshd,nshe->nhde", key_heads, value_heads, preferred_element_type=jnp.float32
    )
    totals = jnp.sum(states, axis=0)
    earlier_sum = exclusive_prefix(totals, "ctx", ctx_devices)

    query_heads = project(0)
    scores = jnp.einsum(
        "nshd,nthd->nhst", query_heads, key_heads, preferred_element_type=jnp.float32
    )
    causal = jnp.arange(SPAN)[:, None] >= jnp.arange(SPAN)[None, :]
    scores = jnp.where(causal[None, None], scores, 0.0).astype(jnp.bfloat16)
    within = jnp.einsum("nhst,nthe->nshe", scores, value_heads, preferred_element_type=jnp.float32)

    prefixes = [earlier_sum]
    for n in range(1, nblk):
        prefixes.append(prefixes[-1] + states[n - 1])
    prefix = jnp.stack(prefixes, axis=0)
    prefix_hi = prefix.astype(jnp.bfloat16)
    prefix_lo = (prefix - prefix_hi.astype(jnp.float32)).astype(jnp.bfloat16)
    carried_out = jnp.einsum(
        "nshd,nhde->nshe", query_heads, prefix_hi, preferred_element_type=jnp.float32
    ) + jnp.einsum(
        "nshd,nhde->nshe", query_heads, prefix_lo, preferred_element_type=jnp.float32
    )
    combined = within + carried_out
    mean_sq = jnp.mean(combined * combined, axis=-1, keepdims=True)
    normed = combined * lax.rsqrt(mean_sq + epsilon) * head_gain
    attn = normed.astype(jnp.bfloat16).reshape(tok_rows, PHM * col_width)
    partial_value = jnp.dot(attn, w_out, preferred_element_type=jnp.float32)
    reduced = lax.psum_scatter(
        partial_value.astype(jnp.bfloat16),
        "tp",
        scatter_dimension=1,
        tiled=True,
    )
    return reduced


def solution(mesh):
    placed = (P("ctx", "tp"), P(None, None, None, "tp"), P(None, "tp", None), P(), P(None, "tp"))
    return jax.shard_map(
        functools.partial(on_device, mesh.shape["ctx"]),
        mesh=mesh,
        in_specs=placed,
        out_specs=P("ctx", "tp"),
        check_vma=False,
    )
```

```python
import functools

import jax
import jax.numpy as jnp
from jax import lax
from jax.sharding import PartitionSpec as P

PHM = 4
SPAN = 128
HEAD = 128
BLOCK = 1024


epsilon = 1e-06


def ring_gather(value, axis, devices, size, stride):
    here = lax.axis_index(axis)
    slots = [value]
    for shift in range(1, size):
        pairs = []
        for i in range(devices):
            k = (i // stride) % size
            pairs.append((i, i + ((k + shift) % size - k) * stride))
        slots.append(lax.ppermute(value, axis, pairs))
    source = ((here // stride) % size - jnp.arange(size)) % size
    return jnp.stack(slots).astype(jnp.float32), source


def exclusive_prefix(value, axis, devices, row):
    here = lax.axis_index(axis)
    pos, col = here % row, here // row
    within, source = ring_gather(value.astype(jnp.bfloat16), axis, devices, row, 1)
    before = jnp.einsum("k,k...->...", (source < pos).astype(jnp.float32), within)
    row_total = jnp.sum(within, axis=0)
    cols = devices // row
    across, source = ring_gather(row_total.astype(jnp.bfloat16), axis, devices, cols, row)
    return before + jnp.einsum("k,k...->...", (source < col).astype(jnp.float32), across)


def fold_weights(blocks, mixing):
    terms, rows, cols = blocks.shape
    folded = None
    for term_index in range(terms):
        part = (
            mixing[term_index][:, None, :, None]
            * blocks[term_index].astype(jnp.float32)[None, :, None, :]
        )
        folded = part if folded is None else folded + part
    return folded.astype(jnp.bfloat16).reshape(PHM * rows, PHM * cols)


def on_device(ctx_devices, ctx_row, tokens, qkv_blocks, out_blocks, mix_factors, head_gain):
    col_width = qkv_blocks.shape[-1]
    w_qkv = jnp.concatenate(
        [fold_weights(qkv_blocks[p], mix_factors[p]) for p in range(3)], axis=1
    )
    w_out = fold_weights(out_blocks, mix_factors[3])

    whole = lax.all_gather(tokens, "tp", axis=1, tiled=True)
    tok_rows = whole.shape[0]
    local_heads = PHM * col_width // HEAD
    nblk = tok_rows // SPAN
    qkv = jnp.dot(whole, w_qkv, preferred_element_type=jnp.float32).astype(jnp.bfloat16)

    def project(p):
        part = qkv[:, p * PHM * col_width:(p + 1) * PHM * col_width]
        return part.reshape(nblk, SPAN, local_heads, HEAD)

    key_heads = project(1)
    value_heads = project(2)
    states = jnp.einsum(
        "nshd,nshe->nhde", key_heads, value_heads, preferred_element_type=jnp.float32
    )
    totals = jnp.sum(states, axis=0)
    earlier_sum = exclusive_prefix(totals, "ctx", ctx_devices, ctx_row)

    query_heads = project(0)
    scores = jnp.einsum(
        "nshd,nthd->nhst", query_heads, key_heads, preferred_element_type=jnp.float32
    )
    causal = jnp.arange(SPAN)[:, None] >= jnp.arange(SPAN)[None, :]
    scores = jnp.where(causal[None, None], scores, 0.0).astype(jnp.bfloat16)
    within = jnp.einsum("nhst,nthe->nshe", scores, value_heads, preferred_element_type=jnp.float32)

    prefixes = [earlier_sum]
    for n in range(1, nblk):
        prefixes.append(prefixes[-1] + states[n - 1])
    prefix = jnp.stack(prefixes, axis=0)
    prefix_hi = prefix.astype(jnp.bfloat16)
    prefix_lo = (prefix - prefix_hi.astype(jnp.float32)).astype(jnp.bfloat16)
    carried_out = jnp.einsum(
        "nshd,nhde->nshe", query_heads, prefix_hi, preferred_element_type=jnp.float32
    ) + jnp.einsum(
        "nshd,nhde->nshe", query_heads, prefix_lo, preferred_element_type=jnp.float32
    )
    combined = within + carried_out
    mean_sq = jnp.mean(combined * combined, axis=-1, keepdims=True)
    normed = combined * lax.rsqrt(mean_sq + epsilon) * head_gain
    attn = normed.astype(jnp.bfloat16).reshape(tok_rows, PHM * col_width)
    partial_value = jnp.dot(attn, w_out, preferred_element_type=jnp.float32)
    reduced = lax.psum_scatter(
        partial_value.astype(jnp.bfloat16),
        "tp",
        scatter_dimension=1,
        tiled=True,
    )
    return reduced


def ctx_row_of(mesh):
    n = mesh.shape["ctx"]
    return 8 if n % 8 == 0 else n


def solution(mesh):
    placed = (P("ctx", "tp"), P(None, None, None, "tp"), P(None, "tp", None), P(), P(None, "tp"))
    return jax.shard_map(
        functools.partial(on_device, mesh.shape["ctx"], ctx_row_of(mesh)),
        mesh=mesh,
        in_specs=placed,
        out_specs=P("ctx", "tp"),
        check_vma=False,
    )
```

```python
import functools

import jax
import jax.numpy as jnp
from jax import lax
from jax.sharding import PartitionSpec as P

PHM = 4
SPAN = 128
HEAD = 128
BLOCK = 1024


epsilon = 1e-06


def ring_gather(value, axis, devices, size, stride):
    here = lax.axis_index(axis)
    slots = [value]
    for shift in range(1, size):
        pairs = []
        for i in range(devices):
            k = (i // stride) % size
            pairs.append((i, i + ((k + shift) % size - k) * stride))
        slots.append(lax.ppermute(value, axis, pairs))
    source = ((here // stride) % size - jnp.arange(size)) % size
    return jnp.stack(slots).astype(jnp.float32), source


def exclusive_prefix(value, axis, devices, row):
    here = lax.axis_index(axis)
    pos, col = here % row, here // row
    within, source = ring_gather(value.astype(jnp.bfloat16), axis, devices, row, 1)
    before = jnp.einsum("k,k...->...", (source < pos).astype(jnp.float32), within)
    row_total = jnp.sum(within, axis=0)
    cols = devices // row
    across, source = ring_gather(row_total.astype(jnp.bfloat16), axis, devices, cols, row)
    return before + jnp.einsum("k,k...->...", (source < col).astype(jnp.float32), across)


def fold_weights(blocks, mixing):
    terms, rows, cols = blocks.shape
    folded = None
    for term_index in range(terms):
        part = (
            mixing[term_index][:, None, :, None]
            * blocks[term_index].astype(jnp.float32)[None, :, None, :]
        )
        folded = part if folded is None else folded + part
    return folded.astype(jnp.bfloat16).reshape(PHM * rows, PHM * cols)


def on_device(ctx_devices, ctx_row, tokens, qkv_blocks, out_blocks, mix_factors, head_gain):
    col_width = qkv_blocks.shape[-1]
    w_kv = jnp.concatenate(
        [fold_weights(qkv_blocks[p], mix_factors[p]) for p in (1, 2)], axis=1
    )
    w_q = fold_weights(qkv_blocks[0], mix_factors[0])
    w_out = fold_weights(out_blocks, mix_factors[3])

    whole = lax.all_gather(tokens, "tp", axis=1, tiled=True)
    tok_rows = whole.shape[0]
    local_heads = PHM * col_width // HEAD
    nblk = tok_rows // SPAN
    width = PHM * col_width
    kv = jnp.dot(whole, w_kv, preferred_element_type=jnp.float32).astype(jnp.bfloat16)
    key_heads = kv[:, :width].reshape(nblk, SPAN, local_heads, HEAD)
    value_heads = kv[:, width:].reshape(nblk, SPAN, local_heads, HEAD)
    states = jnp.einsum(
        "nshd,nshe->nhde", key_heads, value_heads, preferred_element_type=jnp.float32
    )
    totals = jnp.sum(states, axis=0)
    earlier_sum = exclusive_prefix(totals, "ctx", ctx_devices, ctx_row)

    query = jnp.dot(whole, w_q, preferred_element_type=jnp.float32).astype(jnp.bfloat16)
    query_heads = query.reshape(nblk, SPAN, local_heads, HEAD)
    scores = jnp.einsum(
        "nshd,nthd->nhst", query_heads, key_heads, preferred_element_type=jnp.float32
    )
    causal = jnp.arange(SPAN)[:, None] >= jnp.arange(SPAN)[None, :]
    scores = jnp.where(causal[None, None], scores, 0.0).astype(jnp.bfloat16)
    within = jnp.einsum("nhst,nthe->nshe", scores, value_heads, preferred_element_type=jnp.float32)

    prefixes = [earlier_sum]
    for n in range(1, nblk):
        prefixes.append(prefixes[-1] + states[n - 1])
    prefix = jnp.stack(prefixes, axis=0)
    prefix_hi = prefix.astype(jnp.bfloat16)
    prefix_lo = (prefix - prefix_hi.astype(jnp.float32)).astype(jnp.bfloat16)
    carried_out = jnp.einsum(
        "nshd,nhde->nshe", query_heads, prefix_hi, preferred_element_type=jnp.float32
    ) + jnp.einsum(
        "nshd,nhde->nshe", query_heads, prefix_lo, preferred_element_type=jnp.float32
    )
    combined = within + carried_out
    mean_sq = jnp.mean(combined * combined, axis=-1, keepdims=True)
    normed = combined * lax.rsqrt(mean_sq + epsilon) * head_gain
    attn = normed.astype(jnp.bfloat16).reshape(tok_rows, PHM * col_width)
    halves = []
    half = tok_rows // 2
    for part in range(2):
        rows = attn[part * half:(part + 1) * half]
        partial_value = jnp.dot(rows, w_out, preferred_element_type=jnp.float32)
        halves.append(
            lax.psum_scatter(
                partial_value.astype(jnp.bfloat16), "tp", scatter_dimension=1, tiled=True
            )
        )
    reduced = jnp.concatenate(halves, axis=0)
    return reduced


def ctx_row_of(mesh):
    n = mesh.shape["ctx"]
    return 8 if n % 8 == 0 else n


def solution(mesh):
    placed = (P("ctx", "tp"), P(None, None, None, "tp"), P(None, "tp", None), P(), P(None, "tp"))
    return jax.shard_map(
        functools.partial(on_device, mesh.shape["ctx"], ctx_row_of(mesh)),
        mesh=mesh,
        in_specs=placed,
        out_specs=P("ctx", "tp"),
        check_vma=False,
    )
```

```python
import functools

import jax
import jax.numpy as jnp
from jax import lax
from jax.sharding import PartitionSpec as P

PHM = 4
SPAN = 128
HEAD = 128
BLOCK = 1024


epsilon = 1e-06


def ring_gather(value, axis, devices, size, stride, before):
    here = lax.axis_index(axis)
    k_here = (here // stride) % size
    total = value.astype(jnp.float32)
    earlier = jnp.zeros_like(total)
    for shift in range(1, size):
        pairs = []
        for i in range(devices):
            k = (i // stride) % size
            pairs.append((i, i + ((k + shift) % size - k) * stride))
        got = lax.ppermute(value, axis, pairs).astype(jnp.float32)
        source = (k_here - shift) % size
        total = total + got
        earlier = earlier + jnp.where(source < before, got, 0.0)
    return total, earlier


def exclusive_prefix(value, axis, devices, row):
    here = lax.axis_index(axis)
    pos, col = here % row, here // row
    row_total, before = ring_gather(value.astype(jnp.bfloat16), axis, devices, row, 1, pos)
    _, rows_before = ring_gather(row_total, axis, devices, devices // row, row, col)
    return before + rows_before


def fold_weights(blocks, mixing):
    projections, terms, rows, cols = blocks.shape
    folded = None
    for term_index in range(terms):
        mix = jnp.transpose(mixing[:, term_index], (1, 0, 2))[:, None, :, :, None]
        block = jnp.transpose(blocks[:, term_index].astype(jnp.float32), (1, 0, 2))
        part = mix * block[None, :, :, None, :]
        folded = part if folded is None else folded + part
    return folded.astype(jnp.bfloat16).reshape(PHM * rows, projections * PHM * cols)


def on_device(ctx_devices, ctx_row, tokens, qkv_blocks, out_blocks, mix_factors, head_gain):
    col_width = qkv_blocks.shape[-1]
    w_kv, w_q, w_out = lax.optimization_barrier(
        (
            fold_weights(qkv_blocks[1:], mix_factors[1:3]),
            fold_weights(qkv_blocks[:1], mix_factors[:1]),
            fold_weights(out_blocks[None], mix_factors[3:]),
        )
    )

    whole = lax.all_gather(tokens, "tp", axis=1, tiled=True)
    tok_rows = whole.shape[0]
    local_heads = PHM * col_width // HEAD
    nblk = tok_rows // SPAN
    width = PHM * col_width
    kv = jnp.dot(whole, w_kv, preferred_element_type=jnp.float32).astype(jnp.bfloat16)
    key_heads = kv[:, :width].reshape(nblk, SPAN, local_heads, HEAD)
    value_heads = kv[:, width:].reshape(nblk, SPAN, local_heads, HEAD)
    states = jnp.einsum(
        "nshd,nshe->nhde", key_heads, value_heads, preferred_element_type=jnp.float32
    )
    totals = jnp.sum(states, axis=0)
    earlier_sum = exclusive_prefix(totals, "ctx", ctx_devices, ctx_row)

    query = jnp.dot(whole, w_q, preferred_element_type=jnp.float32).astype(jnp.bfloat16)
    query_heads = query.reshape(nblk, SPAN, local_heads, HEAD)
    scores = jnp.einsum(
        "nshd,nthd->nhst", query_heads, key_heads, preferred_element_type=jnp.float32
    )
    causal = jnp.arange(SPAN)[:, None] >= jnp.arange(SPAN)[None, :]
    scores = jnp.where(causal[None, None], scores, 0.0).astype(jnp.bfloat16)
    within = jnp.einsum("nhst,nthe->nshe", scores, value_heads, preferred_element_type=jnp.float32)

    prefixes = [earlier_sum]
    for n in range(1, nblk):
        prefixes.append(prefixes[-1] + states[n - 1])
    prefix = jnp.stack(prefixes, axis=0)
    prefix_hi = prefix.astype(jnp.bfloat16)
    prefix_lo = (prefix - prefix_hi.astype(jnp.float32)).astype(jnp.bfloat16)
    carried_out = jnp.einsum(
        "nshd,nhde->nshe",
        jnp.concatenate([query_heads, query_heads], axis=-1),
        jnp.concatenate([prefix_hi, prefix_lo], axis=-2),
        preferred_element_type=jnp.float32,
    )
    combined = within + carried_out
    mean_sq = jnp.mean(combined * combined, axis=-1, keepdims=True)
    normed = combined * lax.rsqrt(mean_sq + epsilon) * head_gain
    attn = normed.astype(jnp.bfloat16).reshape(tok_rows, PHM * col_width)
    attn = lax.optimization_barrier(attn)
    partial_value = jnp.dot(attn, w_out, preferred_element_type=jnp.float32)
    reduced = lax.psum_scatter(
        partial_value.astype(jnp.bfloat16),
        "tp",
        scatter_dimension=1,
        tiled=True,
    )
    return reduced


def ctx_row_of(mesh):
    n = mesh.shape["ctx"]
    return 8 if n % 8 == 0 else n


def solution(mesh):
    placed = (P("ctx", "tp"), P(None, None, None, "tp"), P(None, "tp", None), P(), P(None, "tp"))
    return jax.shard_map(
        functools.partial(on_device, mesh.shape["ctx"], ctx_row_of(mesh)),
        mesh=mesh,
        in_specs=placed,
        out_specs=P("ctx", "tp"),
        check_vma=False,
    )
```

```python
import functools

import jax
import jax.numpy as jnp
from jax import lax
from jax.sharding import PartitionSpec as P

PHM = 4
SPAN = 128
HEAD = 128
BLOCK = 1024


epsilon = 1e-06


def ring_gather(value, axis, devices, size, stride, before):
    here = lax.axis_index(axis)
    k_here = (here // stride) % size
    total = value.astype(jnp.float32)
    earlier = jnp.zeros_like(total)
    for shift in range(1, size):
        pairs = []
        for i in range(devices):
            k = (i // stride) % size
            pairs.append((i, i + ((k + shift) % size - k) * stride))
        got = lax.ppermute(value, axis, pairs).astype(jnp.float32)
        source = (k_here - shift) % size
        total = total + got
        earlier = earlier + jnp.where(source < before, got, 0.0)
    return total, earlier


def exclusive_prefix(value, axis, devices, row):
    here = lax.axis_index(axis)
    pos, col = here % row, here // row
    row_total, before = ring_gather(value.astype(jnp.bfloat16), axis, devices, row, 1, pos)
    _, rows_before = ring_gather(row_total, axis, devices, devices // row, row, col)
    return before + rows_before


def fold_weights(blocks, mixing):
    terms, rows, cols = blocks.shape
    folded = None
    for term_index in range(terms):
        part = (
            mixing[term_index][:, None, :, None]
            * blocks[term_index].astype(jnp.float32)[None, :, None, :]
        )
        folded = part if folded is None else folded + part
    return folded.reshape(PHM * rows, PHM * cols)


def split_bf16(value):
    high = value.astype(jnp.bfloat16)
    return high, (value - high.astype(jnp.float32)).astype(jnp.bfloat16)


def project(whole, parts):
    high, low = parts
    out = jnp.dot(whole, high, preferred_element_type=jnp.float32)
    out = out + jnp.dot(whole, low, preferred_element_type=jnp.float32)
    return out.astype(jnp.bfloat16)


def on_device(ctx_devices, ctx_row, tokens, qkv_blocks, out_blocks, mix_factors, head_gain):
    col_width = qkv_blocks.shape[-1]
    w_kv = split_bf16(
        jnp.concatenate([fold_weights(qkv_blocks[p], mix_factors[p]) for p in (1, 2)], axis=1)
    )
    w_q = split_bf16(fold_weights(qkv_blocks[0], mix_factors[0]))
    w_out = fold_weights(out_blocks, mix_factors[3]).astype(jnp.bfloat16)

    whole = lax.all_gather(tokens, "tp", axis=1, tiled=True)
    tok_rows = whole.shape[0]
    local_heads = PHM * col_width // HEAD
    nblk = tok_rows // SPAN
    width = PHM * col_width
    kv = project(whole, w_kv)
    key_heads = kv[:, :width].reshape(nblk, SPAN, local_heads, HEAD)
    value_heads = kv[:, width:].reshape(nblk, SPAN, local_heads, HEAD)
    states = jnp.einsum(
        "nshd,nshe->nhde", key_heads, value_heads, preferred_element_type=jnp.float32
    )
    totals = jnp.sum(states, axis=0)
    earlier_sum = exclusive_prefix(totals, "ctx", ctx_devices, ctx_row)

    query = project(whole, w_q)
    query_heads = query.reshape(nblk, SPAN, local_heads, HEAD)
    scores = jnp.einsum(
        "nshd,nthd->nhst", query_heads, key_heads, preferred_element_type=jnp.float32
    )
    causal = jnp.arange(SPAN)[:, None] >= jnp.arange(SPAN)[None, :]
    scores = jnp.where(causal[None, None], scores, 0.0).astype(jnp.bfloat16)
    within = jnp.einsum("nhst,nthe->nshe", scores, value_heads, preferred_element_type=jnp.float32)

    prefixes = [earlier_sum]
    for n in range(1, nblk):
        prefixes.append(prefixes[-1] + states[n - 1])
    prefix = jnp.stack(prefixes, axis=0)
    prefix_hi = prefix.astype(jnp.bfloat16)
    prefix_lo = (prefix - prefix_hi.astype(jnp.float32)).astype(jnp.bfloat16)
    carried_out = jnp.einsum(
        "nshd,nhde->nshe",
        jnp.concatenate([query_heads, query_heads], axis=-1),
        jnp.concatenate([prefix_hi, prefix_lo], axis=-2),
        preferred_element_type=jnp.float32,
    )
    combined = within + carried_out
    mean_sq = jnp.mean(combined * combined, axis=-1, keepdims=True)
    normed = combined * lax.rsqrt(mean_sq + epsilon) * head_gain
    attn = normed.astype(jnp.bfloat16).reshape(tok_rows, PHM * col_width)
    partial_value = jnp.dot(attn, w_out, preferred_element_type=jnp.float32)
    reduced = lax.psum_scatter(
        partial_value.astype(jnp.bfloat16),
        "tp",
        scatter_dimension=1,
        tiled=True,
    )
    return reduced


def ctx_row_of(mesh):
    n = mesh.shape["ctx"]
    return 8 if n % 8 == 0 else n


def solution(mesh):
    placed = (P("ctx", "tp"), P(None, None, None, "tp"), P(None, "tp", None), P(), P(None, "tp"))
    return jax.shard_map(
        functools.partial(on_device, mesh.shape["ctx"], ctx_row_of(mesh)),
        mesh=mesh,
        in_specs=placed,
        out_specs=P("ctx", "tp"),
        check_vma=False,
    )
```

```python
import functools

import jax
import jax.numpy as jnp
from jax import lax
from jax.sharding import PartitionSpec as P

PHM = 4
SPAN = 128
HEAD = 128
BLOCK = 1024


epsilon = 1e-06


def ring_gather(value, axis, devices, size, stride, before):
    here = lax.axis_index(axis)
    k_here = (here // stride) % size
    total = value.astype(jnp.float32)
    earlier = jnp.zeros_like(total)
    for shift in range(1, size):
        pairs = []
        for i in range(devices):
            k = (i // stride) % size
            pairs.append((i, i + ((k + shift) % size - k) * stride))
        got = lax.ppermute(value, axis, pairs).astype(jnp.float32)
        source = (k_here - shift) % size
        total = total + got
        earlier = earlier + jnp.where(source < before, got, 0.0)
    return total, earlier


def exclusive_prefix(value, axis, devices, row):
    here = lax.axis_index(axis)
    pos, col = here % row, here // row
    row_total, before = ring_gather(value.astype(jnp.bfloat16), axis, devices, row, 1, pos)
    _, rows_before = ring_gather(row_total, axis, devices, devices // row, row, col)
    return before + rows_before


def fold_weights(blocks, mixing):
    terms, rows, cols = blocks.shape
    folded = None
    for term_index in range(terms):
        part = (
            mixing[term_index][:, None, :, None]
            * blocks[term_index].astype(jnp.float32)[None, :, None, :]
        )
        folded = part if folded is None else folded + part
    return folded.reshape(PHM * rows, PHM * cols)


def project(blocked, blocks, mixing, tok_rows):
    projections, terms, rows, cols = blocks.shape
    weights = jnp.transpose(blocks, (2, 0, 1, 3)).reshape(rows, projections * terms * cols)
    product = jnp.dot(blocked, weights, preferred_element_type=jnp.float32)
    product = product.reshape(tok_rows, PHM, projections, terms, cols)
    outs = []
    for p in range(projections):
        summed = None
        for term_index in range(terms):
            for c in range(PHM):
                part = product[:, c, p, term_index, None, :] * mixing[p, term_index, c][None, :, None]
                summed = part if summed is None else summed + part
        outs.append(summed.astype(jnp.bfloat16).reshape(tok_rows, PHM * cols))
    return outs


def on_device(ctx_devices, ctx_row, tokens, qkv_blocks, out_blocks, mix_factors, head_gain):
    col_width = qkv_blocks.shape[-1]
    w_out = fold_weights(out_blocks, mix_factors[3]).astype(jnp.bfloat16)

    whole = lax.all_gather(tokens, "tp", axis=1, tiled=True)
    tok_rows = whole.shape[0]
    local_heads = PHM * col_width // HEAD
    nblk = tok_rows // SPAN
    width = PHM * col_width
    blocked = whole.reshape(tok_rows * PHM, BLOCK)
    key, value = project(blocked, qkv_blocks[1:], mix_factors[1:3], tok_rows)
    key_heads = key.reshape(nblk, SPAN, local_heads, HEAD)
    value_heads = value.reshape(nblk, SPAN, local_heads, HEAD)
    states = jnp.einsum(
        "nshd,nshe->nhde", key_heads, value_heads, preferred_element_type=jnp.float32
    )
    totals = jnp.sum(states, axis=0)
    earlier_sum = exclusive_prefix(totals, "ctx", ctx_devices, ctx_row)

    (query,) = project(blocked, qkv_blocks[:1], mix_factors[:1], tok_rows)
    query_heads = query.reshape(nblk, SPAN, local_heads, HEAD)
    scores = jnp.einsum(
        "nshd,nthd->nhst", query_heads, key_heads, preferred_element_type=jnp.float32
    )
    causal = jnp.arange(SPAN)[:, None] >= jnp.arange(SPAN)[None, :]
    scores = jnp.where(causal[None, None], scores, 0.0).astype(jnp.bfloat16)
    within = jnp.einsum("nhst,nthe->nshe", scores, value_heads, preferred_element_type=jnp.float32)

    prefixes = [earlier_sum]
    for n in range(1, nblk):
        prefixes.append(prefixes[-1] + states[n - 1])
    prefix = jnp.stack(prefixes, axis=0)
    prefix_hi = prefix.astype(jnp.bfloat16)
    prefix_lo = (prefix - prefix_hi.astype(jnp.float32)).astype(jnp.bfloat16)
    carried_out = jnp.einsum(
        "nshd,nhde->nshe",
        jnp.concatenate([query_heads, query_heads], axis=-1),
        jnp.concatenate([prefix_hi, prefix_lo], axis=-2),
        preferred_element_type=jnp.float32,
    )
    combined = within + carried_out
    mean_sq = jnp.mean(combined * combined, axis=-1, keepdims=True)
    normed = combined * lax.rsqrt(mean_sq + epsilon) * head_gain
    attn = normed.astype(jnp.bfloat16).reshape(tok_rows, PHM * col_width)
    partial_value = jnp.dot(attn, w_out, preferred_element_type=jnp.float32)
    reduced = lax.psum_scatter(
        partial_value.astype(jnp.bfloat16),
        "tp",
        scatter_dimension=1,
        tiled=True,
    )
    return reduced


def ctx_row_of(mesh):
    n = mesh.shape["ctx"]
    return 8 if n % 8 == 0 else n


def solution(mesh):
    placed = (P("ctx", "tp"), P(None, None, None, "tp"), P(None, "tp", None), P(), P(None, "tp"))
    return jax.shard_map(
        functools.partial(on_device, mesh.shape["ctx"], ctx_row_of(mesh)),
        mesh=mesh,
        in_specs=placed,
        out_specs=P("ctx", "tp"),
        check_vma=False,
    )
```

```python
import functools

import jax
import jax.numpy as jnp
from jax import lax
from jax.sharding import PartitionSpec as P

PHM = 4
SPAN = 128
HEAD = 128
BLOCK = 1024


epsilon = 1e-06


def ring_gather(value, axis, devices, size, stride, before):
    here = lax.axis_index(axis)
    k_here = (here // stride) % size
    total = value.astype(jnp.float32)
    earlier = jnp.zeros_like(total)
    for shift in range(1, size):
        pairs = []
        for i in range(devices):
            k = (i // stride) % size
            pairs.append((i, i + ((k + shift) % size - k) * stride))
        got = lax.ppermute(value, axis, pairs).astype(jnp.float32)
        source = (k_here - shift) % size
        total = total + got
        earlier = earlier + jnp.where(source < before, got, 0.0)
    return total, earlier


def exclusive_prefix(value, axis, devices, row):
    here = lax.axis_index(axis)
    pos, col = here % row, here // row
    row_total, before = ring_gather(value.astype(jnp.bfloat16), axis, devices, row, 1, pos)
    _, rows_before = ring_gather(row_total, axis, devices, devices // row, row, col)
    return before + rows_before


def fold_weights(blocks, mixing):
    terms, rows, cols = blocks.shape
    folded = None
    for term_index in range(terms):
        part = (
            mixing[term_index][:, None, :, None]
            * blocks[term_index].astype(jnp.float32)[None, :, None, :]
        )
        folded = part if folded is None else folded + part
    return folded.reshape(PHM * rows, PHM * cols)


def project(whole, blocks, mixing):
    projections, terms, rows, cols = blocks.shape
    tok_rows = whole.shape[0]
    weights = jnp.transpose(blocks, (2, 0, 1, 3)).reshape(rows, projections * terms * cols)
    products = [
        jnp.dot(whole[:, c * rows:(c + 1) * rows], weights, preferred_element_type=jnp.float32)
        for c in range(PHM)
    ]
    outs = []
    for p in range(projections):
        summed = None
        for term_index in range(terms):
            at = (p * terms + term_index) * cols
            for c in range(PHM):
                part = products[c][:, None, at:at + cols] * mixing[p, term_index, c][None, :, None]
                summed = part if summed is None else summed + part
        outs.append(summed.astype(jnp.bfloat16).reshape(tok_rows, PHM * cols))
    return outs


def on_device(ctx_devices, ctx_row, tokens, qkv_blocks, out_blocks, mix_factors, head_gain):
    col_width = qkv_blocks.shape[-1]
    w_out = fold_weights(out_blocks, mix_factors[3]).astype(jnp.bfloat16)

    whole = lax.all_gather(tokens, "tp", axis=1, tiled=True)
    tok_rows = whole.shape[0]
    local_heads = PHM * col_width // HEAD
    nblk = tok_rows // SPAN
    width = PHM * col_width
    key, value = project(whole, qkv_blocks[1:], mix_factors[1:3])
    key_heads = key.reshape(nblk, SPAN, local_heads, HEAD)
    value_heads = value.reshape(nblk, SPAN, local_heads, HEAD)
    states = jnp.einsum(
        "nshd,nshe->nhde", key_heads, value_heads, preferred_element_type=jnp.float32
    )
    totals = jnp.sum(states, axis=0)
    earlier_sum = exclusive_prefix(totals, "ctx", ctx_devices, ctx_row)

    (query,) = project(whole, qkv_blocks[:1], mix_factors[:1])
    query_heads = query.reshape(nblk, SPAN, local_heads, HEAD)
    scores = jnp.einsum(
        "nshd,nthd->nhst", query_heads, key_heads, preferred_element_type=jnp.float32
    )
    causal = jnp.arange(SPAN)[:, None] >= jnp.arange(SPAN)[None, :]
    scores = jnp.where(causal[None, None], scores, 0.0).astype(jnp.bfloat16)
    within = jnp.einsum("nhst,nthe->nshe", scores, value_heads, preferred_element_type=jnp.float32)

    prefixes = [earlier_sum]
    for n in range(1, nblk):
        prefixes.append(prefixes[-1] + states[n - 1])
    prefix = jnp.stack(prefixes, axis=0)
    prefix_hi = prefix.astype(jnp.bfloat16)
    prefix_lo = (prefix - prefix_hi.astype(jnp.float32)).astype(jnp.bfloat16)
    carried_out = jnp.einsum(
        "nshd,nhde->nshe",
        jnp.concatenate([query_heads, query_heads], axis=-1),
        jnp.concatenate([prefix_hi, prefix_lo], axis=-2),
        preferred_element_type=jnp.float32,
    )
    combined = within + carried_out
    mean_sq = jnp.mean(combined * combined, axis=-1, keepdims=True)
    normed = combined * lax.rsqrt(mean_sq + epsilon) * head_gain
    attn = normed.astype(jnp.bfloat16).reshape(tok_rows, PHM * col_width)
    partial_value = jnp.dot(attn, w_out, preferred_element_type=jnp.float32)
    reduced = lax.psum_scatter(
        partial_value.astype(jnp.bfloat16),
        "tp",
        scatter_dimension=1,
        tiled=True,
    )
    return reduced


def ctx_row_of(mesh):
    n = mesh.shape["ctx"]
    return 8 if n % 8 == 0 else n


def solution(mesh):
    placed = (P("ctx", "tp"), P(None, None, None, "tp"), P(None, "tp", None), P(), P(None, "tp"))
    return jax.shard_map(
        functools.partial(on_device, mesh.shape["ctx"], ctx_row_of(mesh)),
        mesh=mesh,
        in_specs=placed,
        out_specs=P("ctx", "tp"),
        check_vma=False,
    )
```

```python
import functools

import jax
import jax.numpy as jnp
from jax import lax
from jax.sharding import PartitionSpec as P

PHM = 4
SPAN = 128
HEAD = 128
BLOCK = 1024


epsilon = 1e-06


def ring_gather(value, axis, devices, size, stride, before):
    here = lax.axis_index(axis)
    k_here = (here // stride) % size
    total = value.astype(jnp.float32)
    earlier = jnp.zeros_like(total)
    for shift in range(1, size):
        pairs = []
        for i in range(devices):
            k = (i // stride) % size
            pairs.append((i, i + ((k + shift) % size - k) * stride))
        got = lax.ppermute(value, axis, pairs).astype(jnp.float32)
        source = (k_here - shift) % size
        total = total + got
        earlier = earlier + jnp.where(source < before, got, 0.0)
    return total, earlier


def exclusive_prefix(value, axis, devices, row):
    here = lax.axis_index(axis)
    pos, col = here % row, here // row
    row_total, before = ring_gather(value.astype(jnp.bfloat16), axis, devices, row, 1, pos)
    _, rows_before = ring_gather(row_total, axis, devices, devices // row, row, col)
    return before + rows_before


def fold_weights(blocks, mixing):
    terms, rows, cols = blocks.shape
    folded = None
    for term_index in range(terms):
        part = (
            mixing[term_index][:, None, :, None]
            * blocks[term_index].astype(jnp.float32)[None, :, None, :]
        )
        folded = part if folded is None else folded + part
    return folded.reshape(PHM * rows, PHM * cols)


def project(whole, blocks, mixing):
    projections, terms, rows, cols = blocks.shape
    tok_rows = whole.shape[0]
    weights = jnp.transpose(blocks, (2, 0, 1, 3)).reshape(rows, projections * terms * cols)
    products = [
        jnp.dot(whole[:, c * rows:(c + 1) * rows], weights, preferred_element_type=jnp.float32)
        for c in range(PHM)
    ]
    outs = []
    for p in range(projections):
        summed = None
        for term_index in range(terms):
            at = (p * terms + term_index) * cols
            for c in range(PHM):
                part = products[c][:, None, at:at + cols] * mixing[p, term_index, c][None, :, None]
                summed = part if summed is None else summed + part
        outs.append(summed.astype(jnp.bfloat16).reshape(tok_rows, PHM * cols))
    return lax.optimization_barrier(outs)


def on_device(ctx_devices, ctx_row, tokens, qkv_blocks, out_blocks, mix_factors, head_gain):
    col_width = qkv_blocks.shape[-1]
    w_out = fold_weights(out_blocks, mix_factors[3]).astype(jnp.bfloat16)

    whole = lax.all_gather(tokens, "tp", axis=1, tiled=True)
    tok_rows = whole.shape[0]
    local_heads = PHM * col_width // HEAD
    nblk = tok_rows // SPAN
    width = PHM * col_width
    key, value = project(whole, qkv_blocks[1:], mix_factors[1:3])
    key_heads = key.reshape(nblk, SPAN, local_heads, HEAD)
    value_heads = value.reshape(nblk, SPAN, local_heads, HEAD)
    states = jnp.einsum(
        "nshd,nshe->nhde", key_heads, value_heads, preferred_element_type=jnp.float32
    )
    totals = jnp.sum(states, axis=0)
    earlier_sum = exclusive_prefix(totals, "ctx", ctx_devices, ctx_row)

    (query,) = project(whole, qkv_blocks[:1], mix_factors[:1])
    query_heads = query.reshape(nblk, SPAN, local_heads, HEAD)
    scores = jnp.einsum(
        "nshd,nthd->nhst", query_heads, key_heads, preferred_element_type=jnp.float32
    )
    causal = jnp.arange(SPAN)[:, None] >= jnp.arange(SPAN)[None, :]
    scores = jnp.where(causal[None, None], scores, 0.0).astype(jnp.bfloat16)
    within = jnp.einsum("nhst,nthe->nshe", scores, value_heads, preferred_element_type=jnp.float32)

    prefixes = [earlier_sum]
    for n in range(1, nblk):
        prefixes.append(prefixes[-1] + states[n - 1])
    prefix = jnp.stack(prefixes, axis=0)
    prefix_hi = prefix.astype(jnp.bfloat16)
    prefix_lo = (prefix - prefix_hi.astype(jnp.float32)).astype(jnp.bfloat16)
    carried_out = jnp.einsum(
        "nshd,nhde->nshe",
        jnp.concatenate([query_heads, query_heads], axis=-1),
        jnp.concatenate([prefix_hi, prefix_lo], axis=-2),
        preferred_element_type=jnp.float32,
    )
    combined = within + carried_out
    mean_sq = jnp.mean(combined * combined, axis=-1, keepdims=True)
    normed = combined * lax.rsqrt(mean_sq + epsilon) * head_gain
    attn = normed.astype(jnp.bfloat16).reshape(tok_rows, PHM * col_width)
    partial_value = jnp.dot(attn, w_out, preferred_element_type=jnp.float32)
    reduced = lax.psum_scatter(
        partial_value.astype(jnp.bfloat16),
        "tp",
        scatter_dimension=1,
        tiled=True,
    )
    return reduced


def ctx_row_of(mesh):
    n = mesh.shape["ctx"]
    return 8 if n % 8 == 0 else n


def solution(mesh):
    placed = (P("ctx", "tp"), P(None, None, None, "tp"), P(None, "tp", None), P(), P(None, "tp"))
    return jax.shard_map(
        functools.partial(on_device, mesh.shape["ctx"], ctx_row_of(mesh)),
        mesh=mesh,
        in_specs=placed,
        out_specs=P("ctx", "tp"),
        check_vma=False,
    )
```

```python
import functools

import jax
import jax.numpy as jnp
from jax import lax
from jax.sharding import PartitionSpec as P

PHM = 4
SPAN = 128
HEAD = 128
BLOCK = 1024


epsilon = 1e-06


def ring_gather(value, axis, devices, size, stride, before):
    here = lax.axis_index(axis)
    k_here = (here // stride) % size
    total = value.astype(jnp.float32)
    earlier = jnp.zeros_like(total)
    for shift in range(1, size):
        pairs = []
        for i in range(devices):
            k = (i // stride) % size
            pairs.append((i, i + ((k + shift) % size - k) * stride))
        got = lax.ppermute(value, axis, pairs).astype(jnp.float32)
        source = (k_here - shift) % size
        total = total + got
        earlier = earlier + jnp.where(source < before, got, 0.0)
    return total, earlier


def earlier_rows(value, axis, devices, size, stride):
    earlier = jnp.zeros_like(value)
    for shift in range(1, size):
        pairs = [(i, i + shift * stride) for i in range(devices) if (i // stride) % size + shift < size]
        earlier = earlier + lax.ppermute(value, axis, pairs)
    return earlier


def exclusive_prefix(value, axis, devices, row):
    here = lax.axis_index(axis)
    pos, col = here % row, here // row
    row_total, before = ring_gather(value.astype(jnp.bfloat16), axis, devices, row, 1, pos)
    rows_before = earlier_rows(row_total, axis, devices, devices // row, row)
    return before + rows_before


def fold_weights(blocks, mixing):
    terms, rows, cols = blocks.shape
    folded = None
    for term_index in range(terms):
        part = (
            mixing[term_index][:, None, :, None]
            * blocks[term_index].astype(jnp.float32)[None, :, None, :]
        )
        folded = part if folded is None else folded + part
    return folded.reshape(PHM * rows, PHM * cols)


def project(whole, blocks, mixing):
    projections, terms, rows, cols = blocks.shape
    tok_rows = whole.shape[0]
    weights = jnp.transpose(blocks, (2, 0, 1, 3)).reshape(rows, projections * terms * cols)
    products = [
        jnp.dot(whole[:, c * rows:(c + 1) * rows], weights, preferred_element_type=jnp.float32)
        for c in range(PHM)
    ]
    outs = []
    for p in range(projections):
        summed = None
        for term_index in range(terms):
            at = (p * terms + term_index) * cols
            for c in range(PHM):
                part = products[c][:, None, at:at + cols] * mixing[p, term_index, c][None, :, None]
                summed = part if summed is None else summed + part
        outs.append(summed.astype(jnp.bfloat16).reshape(tok_rows, PHM * cols))
    return lax.optimization_barrier(outs)


def on_device(ctx_devices, ctx_row, tokens, qkv_blocks, out_blocks, mix_factors, head_gain):
    col_width = qkv_blocks.shape[-1]
    w_out = fold_weights(out_blocks, mix_factors[3]).astype(jnp.bfloat16)

    whole = lax.all_gather(tokens, "tp", axis=1, tiled=True)
    tok_rows = whole.shape[0]
    local_heads = PHM * col_width // HEAD
    nblk = tok_rows // SPAN
    width = PHM * col_width
    key, value = project(whole, qkv_blocks[1:], mix_factors[1:3])
    key_heads = key.reshape(nblk, SPAN, local_heads, HEAD)
    value_heads = value.reshape(nblk, SPAN, local_heads, HEAD)
    states = jnp.einsum(
        "nshd,nshe->nhde", key_heads, value_heads, preferred_element_type=jnp.float32
    )
    totals = jnp.sum(states, axis=0)
    earlier_sum = exclusive_prefix(totals, "ctx", ctx_devices, ctx_row)

    (query,) = project(whole, qkv_blocks[:1], mix_factors[:1])
    query_heads = query.reshape(nblk, SPAN, local_heads, HEAD)
    scores = jnp.einsum(
        "nshd,nthd->nhst", query_heads, key_heads, preferred_element_type=jnp.float32
    )
    causal = jnp.arange(SPAN)[:, None] >= jnp.arange(SPAN)[None, :]
    scores = jnp.where(causal[None, None], scores, 0.0).astype(jnp.bfloat16)
    within = jnp.einsum("nhst,nthe->nshe", scores, value_heads, preferred_element_type=jnp.float32)

    prefixes = [earlier_sum]
    for n in range(1, nblk):
        prefixes.append(prefixes[-1] + states[n - 1])
    prefix = jnp.stack(prefixes, axis=0)
    prefix_hi = prefix.astype(jnp.bfloat16)
    prefix_lo = (prefix - prefix_hi.astype(jnp.float32)).astype(jnp.bfloat16)
    carried_out = jnp.einsum(
        "nshd,nhde->nshe",
        jnp.concatenate([query_heads, query_heads], axis=-1),
        jnp.concatenate([prefix_hi, prefix_lo], axis=-2),
        preferred_element_type=jnp.float32,
    )
    combined = within + carried_out
    mean_sq = jnp.mean(combined * combined, axis=-1, keepdims=True)
    normed = combined * lax.rsqrt(mean_sq + epsilon) * head_gain
    attn = normed.astype(jnp.bfloat16).reshape(tok_rows, PHM * col_width)
    partial_value = jnp.dot(attn, w_out, preferred_element_type=jnp.float32)
    reduced = lax.psum_scatter(
        partial_value.astype(jnp.bfloat16),
        "tp",
        scatter_dimension=1,
        tiled=True,
    )
    return reduced


def ctx_row_of(mesh):
    n = mesh.shape["ctx"]
    return 8 if n % 8 == 0 else n


def solution(mesh):
    placed = (P("ctx", "tp"), P(None, None, None, "tp"), P(None, "tp", None), P(), P(None, "tp"))
    return jax.shard_map(
        functools.partial(on_device, mesh.shape["ctx"], ctx_row_of(mesh)),
        mesh=mesh,
        in_specs=placed,
        out_specs=P("ctx", "tp"),
        check_vma=False,
    )
```

```python
import functools

import jax
import jax.numpy as jnp
from jax import lax
from jax.sharding import PartitionSpec as P

PHM = 4
SPAN = 128
HEAD = 128
BLOCK = 1024


epsilon = 1e-06


def ring_gather(value, axis, devices, size, stride, before):
    here = lax.axis_index(axis)
    k_here = (here // stride) % size
    total = value.astype(jnp.float32)
    earlier = jnp.zeros_like(total)
    for shift in range(1, size):
        pairs = []
        for i in range(devices):
            k = (i // stride) % size
            pairs.append((i, i + ((k + shift) % size - k) * stride))
        got = lax.ppermute(value, axis, pairs).astype(jnp.float32)
        source = (k_here - shift) % size
        total = total + got
        earlier = earlier + jnp.where(source < before, got, 0.0)
    return total, earlier


def exclusive_prefix(value, axis, devices, row):
    here = lax.axis_index(axis)
    pos, col = here % row, here // row
    row_total, before = ring_gather(value.astype(jnp.bfloat16), axis, devices, row, 1, pos)
    _, rows_before = ring_gather(row_total, axis, devices, devices // row, row, col)
    return before + rows_before


def fold_weights(blocks, mixing):
    terms, rows, cols = blocks.shape
    folded = None
    for term_index in range(terms):
        part = (
            mixing[term_index][:, None, :, None]
            * blocks[term_index].astype(jnp.float32)[None, :, None, :]
        )
        folded = part if folded is None else folded + part
    return folded.reshape(PHM * rows, PHM * cols)


def project(whole, blocks, mixing):
    projections, terms, rows, cols = blocks.shape
    tok_rows = whole.shape[0]
    weights = jnp.transpose(blocks, (2, 0, 1, 3)).reshape(rows, projections * terms * cols)
    products = [
        jnp.dot(whole[:, c * rows:(c + 1) * rows], weights, preferred_element_type=jnp.float32)
        for c in range(PHM)
    ]
    outs = []
    for p in range(projections):
        blocks_out = []
        for r in range(PHM):
            summed = None
            for term_index in range(terms):
                at = (p * terms + term_index) * cols
                for c in range(PHM):
                    part = products[c][:, at:at + cols] * mixing[p, term_index, c, r]
                    summed = part if summed is None else summed + part
            blocks_out.append(summed.astype(jnp.bfloat16))
        outs.append(jnp.concatenate(blocks_out, axis=1))
    return lax.optimization_barrier(outs)


def on_device(ctx_devices, ctx_row, tokens, qkv_blocks, out_blocks, mix_factors, head_gain):
    col_width = qkv_blocks.shape[-1]
    w_out = fold_weights(out_blocks, mix_factors[3]).astype(jnp.bfloat16)

    whole = lax.all_gather(tokens, "tp", axis=1, tiled=True)
    tok_rows = whole.shape[0]
    local_heads = PHM * col_width // HEAD
    nblk = tok_rows // SPAN
    width = PHM * col_width
    key, value = project(whole, qkv_blocks[1:], mix_factors[1:3])
    key_heads = key.reshape(nblk, SPAN, local_heads, HEAD)
    value_heads = value.reshape(nblk, SPAN, local_heads, HEAD)
    states = jnp.einsum(
        "nshd,nshe->nhde", key_heads, value_heads, preferred_element_type=jnp.float32
    )
    totals = jnp.sum(states, axis=0)
    earlier_sum = exclusive_prefix(totals, "ctx", ctx_devices, ctx_row)

    (query,) = project(whole, qkv_blocks[:1], mix_factors[:1])
    query_heads = query.reshape(nblk, SPAN, local_heads, HEAD)
    scores = jnp.einsum(
        "nshd,nthd->nhst", query_heads, key_heads, preferred_element_type=jnp.float32
    )
    causal = jnp.arange(SPAN)[:, None] >= jnp.arange(SPAN)[None, :]
    scores = jnp.where(causal[None, None], scores, 0.0).astype(jnp.bfloat16)
    within = jnp.einsum("nhst,nthe->nshe", scores, value_heads, preferred_element_type=jnp.float32)

    prefixes = [earlier_sum]
    for n in range(1, nblk):
        prefixes.append(prefixes[-1] + states[n - 1])
    prefix = jnp.stack(prefixes, axis=0)
    prefix_hi = prefix.astype(jnp.bfloat16)
    prefix_lo = (prefix - prefix_hi.astype(jnp.float32)).astype(jnp.bfloat16)
    carried_out = jnp.einsum(
        "nshd,nhde->nshe",
        jnp.concatenate([query_heads, query_heads], axis=-1),
        jnp.concatenate([prefix_hi, prefix_lo], axis=-2),
        preferred_element_type=jnp.float32,
    )
    combined = within + carried_out
    mean_sq = jnp.mean(combined * combined, axis=-1, keepdims=True)
    normed = combined * lax.rsqrt(mean_sq + epsilon) * head_gain
    attn = normed.astype(jnp.bfloat16).reshape(tok_rows, PHM * col_width)
    partial_value = jnp.dot(attn, w_out, preferred_element_type=jnp.float32)
    reduced = lax.psum_scatter(
        partial_value.astype(jnp.bfloat16),
        "tp",
        scatter_dimension=1,
        tiled=True,
    )
    return reduced


def ctx_row_of(mesh):
    n = mesh.shape["ctx"]
    return 8 if n % 8 == 0 else n


def solution(mesh):
    placed = (P("ctx", "tp"), P(None, None, None, "tp"), P(None, "tp", None), P(), P(None, "tp"))
    return jax.shard_map(
        functools.partial(on_device, mesh.shape["ctx"], ctx_row_of(mesh)),
        mesh=mesh,
        in_specs=placed,
        out_specs=P("ctx", "tp"),
        check_vma=False,
    )
```
